256 devices in a mesh: blk: 32 (over y_hi, z, core), col: 8 (over y_lo, x).
Axes of the slice: x: 4, y: 4 (y_hi: 2, y_lo: 2; y = y_hi * 2 + y_lo), z: 8, core: 2. Of those that a mesh axis runs over, the one named last changes fastest.
Arguments:
- a_blocks: float32 [32, 128, 384, 128], P('col', None, 'blk'), may hold values from -6 to 6
- a_mask: int32 [32, 384], P('col', 'blk'), may hold values 0 or 1
- b_blocks: float32 [384, 128, 32, 128], P('blk', None, 'col'), may hold values from -0.0546875 to 0.0546875
- b_mask: int32 [384, 32], P('blk', 'col'), may hold values 0 or 1
- c_mask: int32 [32, 32], P('blk', 'col'), may hold values 0 or 1
Outputs:
- product: float32 [32, 128, 32, 128], P('blk', None, 'col')
The draws below stay inside these ranges and needn't reach their ends.
All inputs are finite; a program needn't handle non-finite values. No bound on the sum of `a_mask` or of `b_mask` or of `c_mask` on one device may be relied on, other than what follows from the above.
Results may differ from the reference program's by a relative error of at most 0.000071.
Values sent between devices are 32-bit elements; how exact they have to be, the bound alone decides.
No kernel may reach another device: no remote copies, remote signals or barrier semaphores. Data moves between devices by JAX's collectives and lax.ppermute only.
A program may use at most 128 MiB of HBM per device.

```python
import jax
import jax.numpy as jnp
from jax import lax

BLOCK = 128
ROWS = 32
KBLOCKS = 384
COLS = 32


def plant(array, rng, least, largest):
    place = [jax.random.randint(jax.random.fold_in(rng, axis), (), 0, length) for axis, length in enumerate(array.shape)]
    widest = array.shape.index(max(array.shape))
    next_to = place[:widest] + [(place[widest] + 1) % array.shape[widest]] + place[widest + 1:]
    return array.at[tuple(place)].set(least).at[tuple(next_to)].set(largest)


def steps_of(key, extent, shards, low, largest):
    factor_of = 1.0
    for axis_at, blocks in shards:
        steps = jax.random.uniform(jax.random.fold_in(jax.random.fold_in(key, 6), axis_at), (blocks,), jnp.float32, low / len(shards), largest / len(shards))
        factor_of = factor_of * jnp.repeat(jnp.exp(steps), extent[axis_at] // blocks).reshape((-1,) + (1,) * (len(extent) - 1 - axis_at))
    return factor_of


def gaussian(own_key, shape, scale, limit, pieces=(), dtype=jnp.bfloat16):
    drawn = jax.random.normal(own_key, shape, jnp.float32) * scale
    if len(pieces) > 0:
        drawn = steps_of(own_key, shape, pieces, -0.22, 0.18) * drawn
    return jnp.clip(drawn, min=-limit, max=limit).astype(dtype)


def setup_inputs(seed: int = 0) -> dict:
    seeds = jax.random.split(jax.random.key(seed), 6)
    a_blocks = gaussian(seeds[0], (ROWS, BLOCK, KBLOCKS, BLOCK), 1.0, 6.0, ((0, 8), (2, 32)), jnp.float32)
    a_mask = plant((jax.random.randint(seeds[1], (ROWS, KBLOCKS), 0, 2) < 1).astype(jnp.int32), jax.random.fold_in(seeds[1], 1), 0, 1)
    b_blocks = gaussian(seeds[2], (KBLOCKS, BLOCK, COLS, BLOCK), (BLOCK * KBLOCKS // 4) ** -0.5, 0.0546875, ((0, 32), (2, 8)), jnp.float32)
    b_mask = plant((jax.random.randint(seeds[3], (KBLOCKS, COLS), 0, 2) < 1).astype(jnp.int32), jax.random.fold_in(seeds[3], 1), 0, 1)
    c_mask = plant((jax.random.randint(seeds[4], (ROWS, COLS), 0, 4) < 3).astype(jnp.int32), jax.random.fold_in(seeds[4], 1), 0, 1)
    return {"a_blocks": a_blocks, "a_mask": a_mask, "b_blocks": b_blocks, "b_mask": b_mask, "c_mask": c_mask}


def reference(a_blocks, a_mask, b_blocks, b_mask, c_mask):
    masked_a = a_blocks * a_mask.astype(jnp.float32)[:, None, :, None]
    masked_b = b_blocks * b_mask.astype(jnp.float32)[:, None, :, None]
    row_count, size_one, inner_count, size_two = masked_a.shape
    flat_a = masked_a.reshape(row_count * size_one, inner_count * size_two)
    flat_b = masked_b.reshape(inner_count * size_two, masked_b.shape[2] * masked_b.shape[3])
    result = jnp.dot(flat_a, flat_b, precision=lax.Precision.HIGHEST, preferred_element_type=jnp.float32)
    result = result.reshape(row_count, size_one, masked_b.shape[2], masked_b.shape[3])
    return result * c_mask.astype(jnp.float32)[:, None, :, None]
```

```python
import jax
import jax.numpy as jnp
from jax import lax
from jax.sharding import Mesh
from jax.sharding import PartitionSpec as P

CHUNKS = 2


def owner_perm(blk, ylo, xs):
    half = blk // 2
    pairs = []
    for i in range(blk):
        hr, t = divmod(i, half)
        for y in range(ylo):
            for x in range(xs):
                src = (i * ylo + y) * xs + x
                dst = ((half * y + t) * ylo + (y ^ hr)) * xs + x
                pairs.append((src, dst))
    return pairs


def shards(a_blocks, a_mask, b_blocks, b_mask, c_mask, *, perm):
    masked_a = a_blocks * a_mask.astype(jnp.float32)[:, None, :, None]
    masked_b = b_blocks * b_mask.astype(jnp.float32)[:, None, :, None]
    rows_a = lax.all_gather(masked_a, "x", axis=0, tiled=True)
    other_b = lax.ppermute(masked_b, "ylo", [(0, 1), (1, 0)])
    rows = rows_a.shape[0] * rows_a.shape[1]
    depth = rows_a.shape[2] * rows_a.shape[3]
    flat_a = rows_a.reshape(rows, depth)
    side = masked_b.shape[3]
    width = masked_b.shape[2] * side
    own_flat = masked_b.reshape(depth, width)
    other_flat = other_b.reshape(depth, width)
    step = width // CHUNKS
    pieces = []
    for c in range(CHUNKS):
        parts = []
        for src in (own_flat, other_flat):
            part = jnp.dot(
                flat_a,
                src[:, c * step:(c + 1) * step],
                precision=lax.Precision.HIGHEST,
                preferred_element_type=jnp.float32,
            )
            parts.append(part.reshape(rows_a.shape[0], rows_a.shape[1], step // side, side))
        stacked = jnp.concatenate(parts, axis=0)
        pieces.append(lax.psum_scatter(stacked, "blk", scatter_dimension=0, tiled=True))
    owned = jnp.concatenate(pieces, axis=2)
    owned = lax.ppermute(owned, ("blk", "ylo", "x"), perm)
    return owned * c_mask.astype(jnp.float32)[:, None, :, None]


def solution(mesh):
    blk = mesh.shape["blk"]
    col = mesh.shape["col"]
    xs = 4
    ylo = col // xs
    sub = Mesh(mesh.devices.reshape(blk, ylo, xs), ("blk", "ylo", "x"))
    perm = owner_perm(blk, ylo, xs)
    cols = ("ylo", "x")

    def body(a_blocks, a_mask, b_blocks, b_mask, c_mask):
        return shards(a_blocks, a_mask, b_blocks, b_mask, c_mask, perm=perm)

    return jax.shard_map(
        body,
        mesh=sub,
        in_specs=(
            P(cols, None, "blk", None),
            P(cols, "blk"),
            P("blk", None, cols, None),
            P("blk", cols),
            P("blk", cols),
        ),
        out_specs=P("blk", None, cols, None),
        check_vma=False,
    )
```

```python
import jax
import jax.numpy as jnp
from jax import lax
from jax.sharding import Mesh
from jax.sharding import PartitionSpec as P

AXES = ("yhi", "z", "core", "ylo", "x")


def owner_perm(yhis, zs, cores, ylos, xs):
    def linear(yhi, z, c, ylo, x):
        return (((yhi * zs + z) * cores + c) * ylos + ylo) * xs + x

    half = yhis * zs * cores // ylos
    pairs = []
    for yhi in range(yhis):
        for z in range(zs):
            for c in range(cores):
                for ylo in range(ylos):
                    for x in range(xs):
                        t = yhis * z + yhi
                        dst_blk = half * ylo + t
                        dyhi, rest = divmod(dst_blk, zs * cores)
                        dz, dc = divmod(rest, cores)
                        pairs.append((linear(yhi, z, c, ylo, x), linear(dyhi, dz, dc, ylo ^ c, x)))
    return pairs


def shards(a_blocks, a_mask, b_blocks, b_mask, c_mask, *, perm):
    masked_a = a_blocks * a_mask.astype(jnp.float32)[:, None, :, None]
    masked_b = b_blocks * b_mask.astype(jnp.float32)[:, None, :, None]
    rows_a = lax.all_gather(masked_a, "x", axis=0, tiled=True)
    other_b = lax.ppermute(masked_b, "ylo", [(0, 1), (1, 0)])
    rows = rows_a.shape[0] * rows_a.shape[1]
    depth = rows_a.shape[2] * rows_a.shape[3]
    flat_a = rows_a.reshape(rows, depth)
    side = masked_b.shape[3]
    width = masked_b.shape[2] * side
    both_b = jnp.stack([masked_b.reshape(depth, width), other_b.reshape(depth, width)])
    core = lax.axis_index("core")
    keep_b = lax.dynamic_index_in_dim(both_b, core, 0, keepdims=False)
    send_b = lax.dynamic_index_in_dim(both_b, 1 - core, 0, keepdims=False)
    shape = (rows_a.shape[0], rows_a.shape[1], masked_b.shape[2], side)

    def product(src):
        part = jnp.dot(flat_a, src, precision=lax.Precision.HIGHEST, preferred_element_type=jnp.float32)
        return part.reshape(shape)

    sent = lax.ppermute(product(send_b), "core", [(0, 1), (1, 0)])
    (kept,) = lax.optimization_barrier((product(keep_b),))
    summed = kept + sent
    summed = lax.psum_scatter(summed, "z", scatter_dimension=0, tiled=True)
    owned = lax.psum_scatter(summed, "yhi", scatter_dimension=0, tiled=True)
    owned = lax.ppermute(owned, AXES, perm)
    return owned * c_mask.astype(jnp.float32)[:, None, :, None]


def solution(mesh):
    blk = mesh.shape["blk"]
    col = mesh.shape["col"]
    yhis, cores, xs = 2, 2, 4
    zs = blk // (yhis * cores)
    ylos = col // xs
    sub = Mesh(mesh.devices.reshape(yhis, zs, cores, ylos, xs), AXES)
    perm = owner_perm(yhis, zs, cores, ylos, xs)
    rows = ("yhi", "z", "core")
    cols = ("ylo", "x")

    def body(a_blocks, a_mask, b_blocks, b_mask, c_mask):
        return shards(a_blocks, a_mask, b_blocks, b_mask, c_mask, perm=perm)

    return jax.shard_map(
        body,
        mesh=sub,
        in_specs=(
            P(cols, None, rows, None),
            P(cols, rows),
            P(rows, None, cols, None),
            P(rows, cols),
            P(rows, cols),
        ),
        out_specs=P(rows, None, cols, None),
        check_vma=False,
    )
```

```python
import jax
import jax.numpy as jnp
from jax import lax
from jax.sharding import Mesh
from jax.sharding import PartitionSpec as P

AXES = ("yhi", "z", "core", "ylo", "x")


def owner_perm(yhis, zs, cores, ylos, xs):
    def linear(yhi, z, c, ylo, x):
        return (((yhi * zs + z) * cores + c) * ylos + ylo) * xs + x

    half = yhis * zs * cores // ylos
    pairs = []
    for yhi in range(yhis):
        for z in range(zs):
            for c in range(cores):
                for ylo in range(ylos):
                    for x in range(xs):
                        t = yhis * z + yhi
                        dst_blk = half * ylo + t
                        dyhi, rest = divmod(dst_blk, zs * cores)
                        dz, dc = divmod(rest, cores)
                        pairs.append((linear(yhi, z, c, ylo, x), linear(dyhi, dz, dc, ylo ^ c, x)))
    return pairs


def shards(a_blocks, a_mask, b_blocks, b_mask, c_mask, *, perm):
    masked_a = a_blocks * a_mask.astype(jnp.float32)[:, None, :, None]
    masked_b = b_blocks * b_mask.astype(jnp.float32)[:, None, :, None]
    rows_a = lax.all_gather(masked_a.transpose(0, 2, 3, 1), "x", axis=0, tiled=True)
    other_b = lax.ppermute(masked_b, "ylo", [(0, 1), (1, 0)])
    depth = rows_a.shape[1] * rows_a.shape[2]
    flat_a = rows_a.reshape(rows_a.shape[0], depth, rows_a.shape[3])
    side = masked_b.shape[3]
    width = masked_b.shape[2] * side
    both_b = jnp.stack([masked_b.reshape(depth, width), other_b.reshape(depth, width)])
    core = lax.axis_index("core")
    keep_b = lax.dynamic_index_in_dim(both_b, core, 0, keepdims=False)
    send_b = lax.dynamic_index_in_dim(both_b, 1 - core, 0, keepdims=False)
    shape = (rows_a.shape[0], rows_a.shape[3], masked_b.shape[2], side)

    def product(src):
        part = jnp.einsum("tka,kn->tan", flat_a, src, precision=lax.Precision.HIGH, preferred_element_type=jnp.float32)
        return part.reshape(shape)

    sent = lax.ppermute(product(send_b), "core", [(0, 1), (1, 0)])
    (kept,) = lax.optimization_barrier((product(keep_b),))
    summed = kept + sent
    summed = lax.psum_scatter(summed, "z", scatter_dimension=0, tiled=True)
    owned = lax.psum_scatter(summed, "yhi", scatter_dimension=0, tiled=True)
    owned = lax.ppermute(owned, AXES, perm)
    return owned * c_mask.astype(jnp.float32)[:, None, :, None]


def solution(mesh):
    blk = mesh.shape["blk"]
    col = mesh.shape["col"]
    yhis, cores, xs = 2, 2, 4
    zs = blk // (yhis * cores)
    ylos = col // xs
    sub = Mesh(mesh.devices.reshape(yhis, zs, cores, ylos, xs), AXES)
    perm = owner_perm(yhis, zs, cores, ylos, xs)
    rows = ("yhi", "z", "core")
    cols = ("ylo", "x")

    def body(a_blocks, a_mask, b_blocks, b_mask, c_mask):
        return shards(a_blocks, a_mask, b_blocks, b_mask, c_mask, perm=perm)

    return jax.shard_map(
        body,
        mesh=sub,
        in_specs=(
            P(cols, None, rows, None),
            P(cols, rows),
            P(rows, None, cols, None),
            P(rows, cols),
            P(rows, cols),
        ),
        out_specs=P(rows, None, cols, None),
        check_vma=False,
    )
```

```python
import jax
import jax.numpy as jnp
from jax import lax
from jax.sharding import Mesh
from jax.sharding import PartitionSpec as P

AXES = ("yhi", "z", "core", "ylo", "x")
K_CHUNKS = 2


def owner_perm(yhis, zs, cores, ylos, xs, flip):
    def linear(yhi, z, c, ylo, x):
        return (((yhi * zs + z) * cores + c) * ylos + ylo) * xs + x

    half = yhis * zs * cores // ylos
    pairs = []
    for yhi in range(yhis):
        for z in range(zs):
            for c in range(cores):
                for ylo in range(ylos):
                    for x in range(xs):
                        t = yhis * z + (yhi ^ flip)
                        dst_blk = half * ylo + t
                        dyhi, rest = divmod(dst_blk, zs * cores)
                        dz, dc = divmod(rest, cores)
                        pairs.append((linear(yhi, z, c, ylo, x), linear(dyhi, dz, dc, ylo ^ c, x)))
    return pairs


def shards(a_blocks, a_mask, b_blocks, b_mask, c_mask, *, perms):
    masked_a = a_blocks * a_mask.astype(jnp.float32)[:, None, :, None]
    masked_b = b_blocks * b_mask.astype(jnp.float32)[:, None, :, None]
    local_a = masked_a.transpose(0, 2, 3, 1)
    other_b = lax.ppermute(masked_b, "ylo", [(0, 1), (1, 0)])
    side = masked_b.shape[3]
    width = masked_b.shape[2] * side
    depth = masked_b.shape[0] * masked_b.shape[1]
    both_b = jnp.stack([masked_b.reshape(depth, width), other_b.reshape(depth, width)])
    core = lax.axis_index("core")
    keep_b = lax.dynamic_index_in_dim(both_b, core, 0, keepdims=False)
    send_b = lax.dynamic_index_in_dim(both_b, 1 - core, 0, keepdims=False)

    step = masked_a.shape[2] // K_CHUNKS
    send_part = keep_part = None
    for c in range(K_CHUNKS):
        rows_a = lax.all_gather(local_a[:, c * step:(c + 1) * step], "x", axis=0, tiled=True)
        flat_a = rows_a.reshape(rows_a.shape[0], step * rows_a.shape[2], rows_a.shape[3])
        lo, hi = c * step * side, (c + 1) * step * side

        def product(src):
            return jnp.einsum("tka,kn->tan", flat_a, src[lo:hi], precision=lax.Precision.HIGH,
                              preferred_element_type=jnp.float32)

        s, k = product(send_b), product(keep_b)
        send_part = s if send_part is None else send_part + s
        keep_part = k if keep_part is None else keep_part + k
    shape = (send_part.shape[0], send_part.shape[1], masked_b.shape[2], side)
    sent = lax.ppermute(send_part.reshape(shape), "core", [(0, 1), (1, 0)])
    (kept,) = lax.optimization_barrier((keep_part.reshape(shape),))
    summed = kept + sent
    summed = lax.psum_scatter(summed, "z", scatter_dimension=0, tiled=True)
    yhi = lax.axis_index("yhi")
    first = lax.dynamic_index_in_dim(summed, yhi, 0, keepdims=True)
    second = lax.dynamic_index_in_dim(summed, 1 - yhi, 0, keepdims=True)
    owned = lax.ppermute(first, AXES, perms[0]) + lax.ppermute(second, AXES, perms[1])
    return owned * c_mask.astype(jnp.float32)[:, None, :, None]


def solution(mesh):
    blk = mesh.shape["blk"]
    col = mesh.shape["col"]
    yhis, cores, xs = 2, 2, 4
    zs = blk // (yhis * cores)
    ylos = col // xs
    sub = Mesh(mesh.devices.reshape(yhis, zs, cores, ylos, xs), AXES)
    perms = [owner_perm(yhis, zs, cores, ylos, xs, flip) for flip in (0, 1)]
    rows = ("yhi", "z", "core")
    cols = ("ylo", "x")

    def body(a_blocks, a_mask, b_blocks, b_mask, c_mask):
        return shards(a_blocks, a_mask, b_blocks, b_mask, c_mask, perms=perms)

    return jax.shard_map(
        body,
        mesh=sub,
        in_specs=(
            P(cols, None, rows, None),
            P(cols, rows),
            P(rows, None, cols, None),
            P(rows, cols),
            P(rows, cols),
        ),
        out_specs=P(rows, None, cols, None),
        check_vma=False,
    )
```

```python
import jax
import jax.numpy as jnp
from jax import lax
from jax.sharding import Mesh
from jax.sharding import PartitionSpec as P

AXES = ("yhi", "z", "core", "ylo", "x")


def owner_perm(yhis, zs, cores, ylos, xs, flip):
    def linear(yhi, z, c, ylo, x):
        return (((yhi * zs + z) * cores + c) * ylos + ylo) * xs + x

    half = yhis * zs * cores // ylos
    rows_per = half // xs
    pairs = []
    for yhi in range(yhis):
        for z in range(zs):
            for c in range(cores):
                for ylo in range(ylos):
                    for x in range(xs):
                        r = yhis * z + (yhi ^ flip)
                        t = rows_per * ((x + r // rows_per) % xs) + r % rows_per
                        dst_blk = half * ylo + t
                        dyhi, rest = divmod(dst_blk, zs * cores)
                        dz, dc = divmod(rest, cores)
                        pairs.append((linear(yhi, z, c, ylo, x), linear(dyhi, dz, dc, ylo ^ c, x)))
    return pairs


def shards(a_blocks, a_mask, b_blocks, b_mask, c_mask, *, perms):
    masked_a = a_blocks * a_mask.astype(jnp.float32)[:, None, :, None]
    masked_b = b_blocks * b_mask.astype(jnp.float32)[:, None, :, None]
    local_a = masked_a.transpose(0, 2, 3, 1)
    other_b = lax.ppermute(masked_b, "ylo", [(0, 1), (1, 0)])
    side = masked_b.shape[3]
    width = masked_b.shape[2] * side
    depth = masked_b.shape[0] * masked_b.shape[1]
    both_b = jnp.stack([masked_b.reshape(depth, width), other_b.reshape(depth, width)])
    core = lax.axis_index("core")
    keep_b = lax.dynamic_index_in_dim(both_b, core, 0, keepdims=False)
    send_b = lax.dynamic_index_in_dim(both_b, 1 - core, 0, keepdims=False)

    rows_a = lax.all_gather(local_a, "x", axis=0)
    xs = rows_a.shape[0]
    x = lax.axis_index("x")
    pieces = [local_a] + [lax.dynamic_index_in_dim(rows_a, (x + d) % xs, 0, keepdims=False) for d in range(1, xs)]

    def product(piece, src):
        flat = piece.reshape(piece.shape[0], depth, piece.shape[3])
        return jnp.einsum("tka,kn->tan", flat, src, precision=lax.Precision.HIGH,
                          preferred_element_type=jnp.float32)

    send_part = jnp.concatenate([product(p, send_b) for p in pieces], axis=0)
    keep_part = jnp.concatenate([product(p, keep_b) for p in pieces], axis=0)
    shape = (send_part.shape[0], send_part.shape[1], masked_b.shape[2], side)
    sent = lax.ppermute(send_part.reshape(shape), "core", [(0, 1), (1, 0)])
    (kept,) = lax.optimization_barrier((keep_part.reshape(shape),))
    summed = kept + sent
    summed = lax.psum_scatter(summed, "z", scatter_dimension=0, tiled=True)
    yhi = lax.axis_index("yhi")
    first = lax.dynamic_index_in_dim(summed, yhi, 0, keepdims=True)
    second = lax.dynamic_index_in_dim(summed, 1 - yhi, 0, keepdims=True)
    owned = lax.ppermute(first, AXES, perms[0]) + lax.ppermute(second, AXES, perms[1])
    return owned * c_mask.astype(jnp.float32)[:, None, :, None]


def solution(mesh):
    blk = mesh.shape["blk"]
    col = mesh.shape["col"]
    yhis, cores, xs = 2, 2, 4
    zs = blk // (yhis * cores)
    ylos = col // xs
    sub = Mesh(mesh.devices.reshape(yhis, zs, cores, ylos, xs), AXES)
    perms = [owner_perm(yhis, zs, cores, ylos, xs, flip) for flip in (0, 1)]
    rows = ("yhi", "z", "core")
    cols = ("ylo", "x")

    def body(a_blocks, a_mask, b_blocks, b_mask, c_mask):
        return shards(a_blocks, a_mask, b_blocks, b_mask, c_mask, perms=perms)

    return jax.shard_map(
        body,
        mesh=sub,
        in_specs=(
            P(cols, None, rows, None),
            P(cols, rows),
            P(rows, None, cols, None),
            P(rows, cols),
            P(rows, cols),
        ),
        out_specs=P(rows, None, cols, None),
        check_vma=False,
    )
```

```python
import jax
import jax.numpy as jnp
from jax import lax
from jax.sharding import Mesh
from jax.sharding import PartitionSpec as P

AXES = ("yhi", "z", "core", "ylo", "x")
K_CHUNKS = 2


def owner_perm(yhis, zs, cores, ylos, xs, flip):
    def linear(yhi, z, c, ylo, x):
        return (((yhi * zs + z) * cores + c) * ylos + ylo) * xs + x

    half = yhis * zs * cores // ylos
    pairs = []
    for yhi in range(yhis):
        for z in range(zs):
            for c in range(cores):
                for ylo in range(ylos):
                    for x in range(xs):
                        t = yhis * z + (yhi ^ flip)
                        dst_blk = half * ylo + t
                        dyhi, rest = divmod(dst_blk, zs * cores)
                        dz, dc = divmod(rest, cores)
                        pairs.append((linear(yhi, z, c, ylo, x), linear(dyhi, dz, dc, ylo ^ c, x)))
    return pairs


def shards(a_blocks, a_mask, b_blocks, b_mask, c_mask, *, perms):
    masked_a = a_blocks * a_mask.astype(jnp.float32)[:, None, :, None]
    masked_b = b_blocks * b_mask.astype(jnp.float32)[:, None, :, None]
    local_a = masked_a.transpose(0, 2, 3, 1)
    other_b = lax.ppermute(masked_b, "ylo", [(0, 1), (1, 0)])
    side = masked_b.shape[3]
    width = masked_b.shape[2] * side
    depth = masked_b.shape[0] * masked_b.shape[1]
    both_b = jnp.stack([masked_b.reshape(depth, width), other_b.reshape(depth, width)])
    core = lax.axis_index("core")
    keep_b = lax.dynamic_index_in_dim(both_b, core, 0, keepdims=False)
    send_b = lax.dynamic_index_in_dim(both_b, 1 - core, 0, keepdims=False)

    step = masked_a.shape[2] // K_CHUNKS
    send_part = keep_part = None
    for c in range(K_CHUNKS):
        rows_a = lax.all_gather(local_a[:, c * step:(c + 1) * step], "x", axis=0, tiled=True)
        flat_a = rows_a.reshape(rows_a.shape[0], step * rows_a.shape[2], rows_a.shape[3])
        lo, hi = c * step * side, (c + 1) * step * side

        def product(src):
            blocks = src[lo:hi].reshape(hi - lo, masked_b.shape[2], side)
            return jnp.einsum("tka,kcd->tacd", flat_a, blocks, precision=lax.Precision.HIGH,
                              preferred_element_type=jnp.float32)

        s, k = product(send_b), product(keep_b)
        send_part = s if send_part is None else send_part + s
        keep_part = k if keep_part is None else keep_part + k
    sent = lax.ppermute(send_part, "core", [(0, 1), (1, 0)])
    (kept,) = lax.optimization_barrier((keep_part,))
    summed = kept + sent
    summed = lax.psum_scatter(summed, "z", scatter_dimension=0, tiled=True)
    yhi = lax.axis_index("yhi")
    first = lax.dynamic_index_in_dim(summed, yhi, 0, keepdims=True)
    second = lax.dynamic_index_in_dim(summed, 1 - yhi, 0, keepdims=True)
    owned = lax.ppermute(first, AXES, perms[0]) + lax.ppermute(second, AXES, perms[1])
    return owned * c_mask.astype(jnp.float32)[:, None, :, None]


def solution(mesh):
    blk = mesh.shape["blk"]
    col = mesh.shape["col"]
    yhis, cores, xs = 2, 2, 4
    zs = blk // (yhis * cores)
    ylos = col // xs
    sub = Mesh(mesh.devices.reshape(yhis, zs, cores, ylos, xs), AXES)
    perms = [owner_perm(yhis, zs, cores, ylos, xs, flip) for flip in (0, 1)]
    rows = ("yhi", "z", "core")
    cols = ("ylo", "x")

    def body(a_blocks, a_mask, b_blocks, b_mask, c_mask):
        return shards(a_blocks, a_mask, b_blocks, b_mask, c_mask, perms=perms)

    return jax.shard_map(
        body,
        mesh=sub,
        in_specs=(
            P(cols, None, rows, None),
            P(cols, rows),
            P(rows, None, cols, None),
            P(rows, cols),
            P(rows, cols),
        ),
        out_specs=P(rows, None, cols, None),
        check_vma=False,
    )
```

```python
import jax
import jax.numpy as jnp
from jax import lax
from jax.sharding import Mesh
from jax.sharding import PartitionSpec as P

AXES = ("yhi", "z", "core", "ylo", "x")
K_CHUNKS = 1


def owner_perm(yhis, zs, cores, ylos, xs, flip):
    def linear(yhi, z, c, ylo, x):
        return (((yhi * zs + z) * cores + c) * ylos + ylo) * xs + x

    half = yhis * zs * cores // ylos
    pairs = []
    for yhi in range(yhis):
        for z in range(zs):
            for c in range(cores):
                for ylo in range(ylos):
                    for x in range(xs):
                        t = yhis * z + (yhi ^ flip)
                        dst_blk = half * ylo + t
                        dyhi, rest = divmod(dst_blk, zs * cores)
                        dz, dc = divmod(rest, cores)
                        pairs.append((linear(yhi, z, c, ylo, x), linear(dyhi, dz, dc, ylo ^ c, x)))
    return pairs


def shards(a_blocks, a_mask, b_blocks, b_mask, c_mask, *, perms):
    masked_a = a_blocks * a_mask.astype(jnp.float32)[:, None, :, None]
    masked_b = b_blocks * b_mask.astype(jnp.float32)[:, None, :, None]
    local_a = masked_a.transpose(0, 2, 3, 1)
    other_b = lax.ppermute(masked_b, "ylo", [(0, 1), (1, 0)])
    side = masked_b.shape[3]
    width = masked_b.shape[2] * side
    depth = masked_b.shape[0] * masked_b.shape[1]
    both_b = jnp.stack([masked_b.reshape(depth, width), other_b.reshape(depth, width)])
    core = lax.axis_index("core")
    keep_b = lax.dynamic_index_in_dim(both_b, core, 0, keepdims=False)
    send_b = lax.dynamic_index_in_dim(both_b, 1 - core, 0, keepdims=False)

    step = masked_a.shape[2] // K_CHUNKS
    send_part = keep_part = None
    for c in range(K_CHUNKS):
        rows_a = lax.all_gather(local_a[:, c * step:(c + 1) * step], "x", axis=0, tiled=True)
        flat_a = rows_a.reshape(rows_a.shape[0], step * rows_a.shape[2], rows_a.shape[3])
        lo, hi = c * step * side, (c + 1) * step * side

        def product(src):
            return jnp.einsum("tka,kn->tan", flat_a, src[lo:hi], precision=lax.Precision.HIGH,
                              preferred_element_type=jnp.float32)

        s, k = product(send_b), product(keep_b)
        send_part = s if send_part is None else send_part + s
        keep_part = k if keep_part is None else keep_part + k
    shape = (send_part.shape[0], send_part.shape[1], masked_b.shape[2], side)
    sent = lax.ppermute(send_part.reshape(shape), "core", [(0, 1), (1, 0)])
    (kept,) = lax.optimization_barrier((keep_part.reshape(shape),))
    summed = kept + sent
    summed = lax.psum_scatter(summed, "z", scatter_dimension=0, tiled=True)
    yhi = lax.axis_index("yhi")
    first = lax.dynamic_index_in_dim(summed, yhi, 0, keepdims=True)
    second = lax.dynamic_index_in_dim(summed, 1 - yhi, 0, keepdims=True)
    owned = lax.ppermute(first, AXES, perms[0]) + lax.ppermute(second, AXES, perms[1])
    return owned * c_mask.astype(jnp.float32)[:, None, :, None]


def solution(mesh):
    blk = mesh.shape["blk"]
    col = mesh.shape["col"]
    yhis, cores, xs = 2, 2, 4
    zs = blk // (yhis * cores)
    ylos = col // xs
    sub = Mesh(mesh.devices.reshape(yhis, zs, cores, ylos, xs), AXES)
    perms = [owner_perm(yhis, zs, cores, ylos, xs, flip) for flip in (0, 1)]
    rows = ("yhi", "z", "core")
    cols = ("ylo", "x")

    def body(a_blocks, a_mask, b_blocks, b_mask, c_mask):
        return shards(a_blocks, a_mask, b_blocks, b_mask, c_mask, perms=perms)

    return jax.shard_map(
        body,
        mesh=sub,
        in_specs=(
            P(cols, None, rows, None),
            P(cols, rows),
            P(rows, None, cols, None),
            P(rows, cols),
            P(rows, cols),
        ),
        out_specs=P(rows, None, cols, None),
        check_vma=False,
    )
```
